512 devices in a mesh: dp: 32 (over z, core), seq: 16 (over y, x).
Axes of the slice: x: 4, y: 4, z: 16, core: 2. Of those that a mesh axis runs over, the one named last changes fastest.
Arguments:
- mixer_in: bfloat16 [131072, 2816], P(('dp', 'seq')), parts along dimension 0, may hold values from -92 to 92
- gate_input: bfloat16 [131072, 2560], P(('dp', 'seq')), parts along dimension 0, may hold values from -6 to 6
- step_raw: bfloat16 [131072, 40], P(('dp', 'seq')), parts along dimension 0, may hold values from -6 to 6
- lengths: int32 [96], P('dp'), parts along dimension 0, may hold values from 1 to 2048, 4096 in all
- deal_order: int32 [512], P('dp'), parts along dimension 0, may hold values from 0 to 15, as said below
- conv_weight: float32 [4, 2816], replicated, may hold values from -3 to 3
- conv_bias: float32 [2816], replicated, may hold values from -3 to 3
- step_bias: float32 [40], replicated, may hold values from -4 to -1
- decay_rate: float32 [40], replicated, may hold values from 0.01 to 2
- skip_gain: float32 [40], replicated, may hold values from 0.5 to 1.5
- norm_gain: float32 [2560], replicated, may hold values from 0.5 to 1.5
Outputs:
- mixed_out: bfloat16 [131072, 2560], P(('dp', 'seq')), parts along dimension 0
- final_states: float32 [96, 2560, 128], P('dp', 'seq'), parts along dimension 0
The draws below stay inside these ranges and needn't reach their ends.
There are 32 independent parts, one for each index of `dp`. The reference program is written for one: setup_inputs(seed, part) draws one part's arguments, and reference() takes and returns one part's arrays. A program takes and returns all parts, laid end to end along the dimension named above; an argument that names none is the same for every part. Nothing has to cross between parts.
Inputs may be any that keep to these rules, and one draw needn't show every extreme that they name: The prompt lengths sum to 4096 and the longest is exactly 2048. `deal_order`: every sequence stretch stands in exactly one dealt slot.
All inputs are finite; a program needn't handle non-finite values.
Results may differ from the reference program's by a relative error of at most 0.005.
Values may be sent and summed in bfloat16 or wider, within the bound.
No kernel may reach another device: no remote copies, remote signals or barrier semaphores. Data moves between devices by JAX's collectives and lax.ppermute only.
A program may use at most 128 MiB of HBM per device.

```python
import math
import jax
import jax.numpy as jnp
import numpy as np
from jax import lax

HEADS = 40
HEAD_DIM = 64
STATE = 128
KERNEL = 4
STRETCH = 256
DOCS = 3
INNER = 2560
CHANNELS = 2816
STREAM = 4096
STRETCHES = 16
LONGEST = 2048


def dealt_slots(key):
    return jax.random.permutation(jax.random.fold_in(key, 31), STRETCHES).astype(jnp.int32)


def draw_deal_order(key, part):
    return dealt_slots(key)


def draw_mixer_in(key, part):
    sign_key = jax.random.fold_in(key, 41)
    noise_key = jax.random.fold_in(key, 43)
    loud_key = jax.random.fold_in(key, 47)
    pattern = 0.6 * jax.random.rademacher(sign_key, (CHANNELS,), dtype=jnp.float32)
    noise = jnp.clip(jax.random.normal(noise_key, (STREAM, CHANNELS), jnp.float32), -4.0, 4.0)
    loud = jnp.exp(jax.random.uniform(loud_key, (STRETCHES, HEADS), jnp.float32, 0.0, math.log(20.0)))
    columns = jnp.concatenate([jnp.repeat(loud, HEAD_DIM, axis=1), jnp.ones((STRETCHES, 2 * STATE), jnp.float32)], 1)
    row_scale = jnp.repeat(columns, STRETCH, axis=0)
    return (row_scale * (pattern[None, :] + noise)).astype(jnp.bfloat16)


def level_of(own_key, shape, pieces, smallest, high):
    def one(position, blocks):
        heights = jax.random.uniform(jax.random.fold_in(jax.random.fold_in(own_key, 6), position), (blocks,), jnp.float32, smallest / len(pieces), high / len(pieces))
        return jnp.repeat(jnp.exp(heights), shape[position] // blocks).reshape((-1,) + (1,) * (len(shape) - position - 1))

    level = one(*pieces[0])
    for cut in pieces[1:]:
        level = level * one(*cut)
    return level


def split_up(amount, total, most, slope):
    weights = [(1 << 20) // math.isqrt(rank ** slope) + 1 for rank in range(2, amount + 1)]
    surplus, counts = total - most - (amount - 1), [1] * (amount - 1)
    while surplus > 0:
        candidates = [i for i in range(amount - 1) if counts[i] < most]
        pool, remaining = sum([weights[i] for i in candidates]), surplus
        for i in candidates:
            addition = min(most - counts[i], max(1, remaining * weights[i] // pool), surplus)
            counts[i] = counts[i] + addition
            surplus = surplus - addition
    return np.array([most] + counts)


def uneven(own_key, number_of, total, most, skew):
    if number_of == 2:
        one = jax.random.randint(own_key, (), max(1, total - most), min(most, total - 1) + 1)
        return jnp.stack([one, total - one])
    tallies = jnp.asarray(split_up(number_of, total, most, skew), jnp.int32)
    couples = (number_of - 1) // 2
    giver, receiver = tallies[1:1 + 2 * couples:2], tallies[2:2 + 2 * couples:2]
    room = jnp.minimum(giver - 1, most - receiver)
    passed = jax.random.randint(jax.random.fold_in(own_key, 1), (couples,), 0, 1 << 20) % (room + 1)
    tallies = tallies.at[1:1 + 2 * couples:2].set(giver - passed).at[2:2 + 2 * couples:2].set(receiver + passed)
    return tallies[jax.random.permutation(jax.random.fold_in(own_key, 2), number_of)]


def scatter_about(own_key, dims, deviation, bound, shards=(), held_as=jnp.bfloat16):
    result = jax.random.normal(own_key, dims, jnp.float32) * deviation
    if len(shards) > 0:
        result = level_of(own_key, dims, shards, -0.22, 0.18) * result
    return jnp.clip(result, min=-bound, max=bound).astype(held_as)


def setup_inputs(seed: int = 0, part: int = 0) -> dict:
    streams_of = jax.random.split(jax.random.key(seed), 12)
    part_splits = jax.random.split(jax.random.fold_in(streams_of[11], part), 12)
    mixer_in = draw_mixer_in(jax.random.fold_in(jax.random.fold_in(streams_of[11], part), 71), part)
    gate_input = scatter_about(part_splits[1], (STREAM, INNER), 1.0, 6.0, ((0, 16),))
    step_raw = scatter_about(part_splits[2], (STREAM, HEADS), 1.0, 6.0, ((0, 16),))
    lengths = uneven(part_splits[3], DOCS, STREAM, LONGEST, 2).astype(jnp.int32)
    deal_order = draw_deal_order(jax.random.fold_in(jax.random.fold_in(streams_of[11], part), 71), part)
    conv_weight = scatter_about(streams_of[5], (KERNEL, CHANNELS), KERNEL ** -0.5, 3.0, (), jnp.float32)
    conv_bias = scatter_about(streams_of[6], (CHANNELS,), 0.5, 3.0, (), jnp.float32)
    step_bias = jnp.clip(jax.random.uniform(streams_of[7], (HEADS,), jnp.float32, -4.0, -1.0), -4.0, -1.0)
    decay_rate = jnp.clip(jnp.exp(jax.random.uniform(streams_of[8], (HEADS,), jnp.float32, math.log(0.01), math.log(2.0))), 0.01, 2.0)
    skip_gain = jnp.clip(jax.random.uniform(streams_of[9], (HEADS,), jnp.float32, 0.5, 1.5), 0.5, 1.5)
    norm_gain = jnp.clip(1.0 + 0.1 * jax.random.normal(streams_of[10], (INNER,), jnp.float32), 0.5, 1.5)
    return dict(mixer_in=mixer_in, gate_input=gate_input, step_raw=step_raw, lengths=lengths, deal_order=deal_order, conv_weight=conv_weight, conv_bias=conv_bias, step_bias=step_bias, decay_rate=decay_rate, skip_gain=skip_gain, norm_gain=norm_gain)


def doc_index(ends, positions):
    return lax.optimization_barrier(jnp.sum((ends[None, :] <= positions[:, None]).astype(jnp.int32), axis=1)).astype(jnp.int32)

def reference(mixer_in, gate_input, step_raw, lengths, deal_order, conv_weight, conv_bias, step_bias, decay_rate, skip_gain, norm_gain):
    inner = HEADS * HEAD_DIM

    def undeal(source):
        blocks = source.reshape((STRETCHES, STRETCH) + source.shape[1:])
        return jnp.zeros_like(blocks).at[deal_order].set(blocks).reshape(source.shape)
    packed_in = undeal(mixer_in)
    packed_gate = undeal(gate_input)
    packed_step = undeal(step_raw)
    positions = jnp.arange(STREAM, dtype=jnp.int32)
    ends = jnp.cumsum(lengths).astype(jnp.int32)
    doc_ids = doc_index(ends, positions)
    padded = jnp.concatenate([jnp.zeros((KERNEL - 1, CHANNELS), jnp.bfloat16), packed_in], 0)
    padded_doc = jnp.concatenate([jnp.full((KERNEL - 1,), -1, jnp.int32), doc_ids], 0)
    accum = jnp.zeros((STREAM, CHANNELS), jnp.float32) + conv_bias
    for offset in range(KERNEL):
        keep = (padded_doc[offset:offset + STREAM] == doc_ids).astype(jnp.float32)
        accum = accum + conv_weight[offset] * padded[offset:offset + STREAM].astype(jnp.float32) * keep[:, None]
    mixed = jax.nn.silu(accum).astype(jnp.bfloat16)
    values = mixed[:, :inner]
    input_map = mixed[:, inner:inner + STATE]
    output_map = mixed[:, inner + STATE:]
    step = jax.nn.softplus(packed_step.astype(jnp.float32) + step_bias)
    log_decay = -decay_rate * step
    running = jnp.cumsum(log_decay, axis=0)
    scaled = (values.astype(jnp.float32) * jnp.repeat(step, HEAD_DIM, axis=1)).astype(jnp.bfloat16)
    stretch_ids = jnp.arange(STRETCHES, dtype=jnp.int32)
    starts = stretch_ids * STRETCH
    base = running[starts] - log_decay[starts]
    stretch_end = running[starts + STRETCH - 1]
    end_doc = doc_ids[starts + STRETCH - 1]
    prev_doc = jnp.where(stretch_ids > 0, doc_ids[jnp.maximum(starts - 1, 0)], -1).astype(jnp.int32)

    def blocked(source):
        return source.reshape((STRETCHES, STRETCH) + source.shape[1:])

    def local_state(inputs):
        scaled_c, keys_c, running_c, doc_c = inputs
        weight = jnp.exp(jnp.where((doc_c == doc_c[-1])[:, None], running_c[-1][None, :] - running_c, -jnp.inf))
        weighted = (scaled_c.astype(jnp.float32) * jnp.repeat(weight, HEAD_DIM, axis=1)).astype(jnp.bfloat16)
        return jnp.dot(weighted.T, keys_c, preferred_element_type=jnp.float32)
    states = lax.map(local_state, (blocked(scaled), blocked(input_map), blocked(running), blocked(doc_ids)))
    allowed = (stretch_ids[None, :] < stretch_ids[:, None]) & (end_doc[None, :] == prev_doc[:, None])
    gaps = jnp.exp(jnp.where(allowed[:, :, None], base[:, None, :] - stretch_end[None, :, :], -jnp.inf))

    def inflow(gap_row):
        return jnp.einsum('ck,ckn->kn', jnp.repeat(gap_row, HEAD_DIM, axis=1), states, precision=lax.Precision.HIGHEST)
    state_in = lax.map(inflow, gaps)
    lane = jnp.arange(STRETCH, dtype=jnp.int32)
    later = lane[:, None] >= lane[None, :]

    def stretch_out(inputs):
        values_c, scaled_c, keys_c, queries_c, running_c, doc_c, base_c, prev_c, state_c = inputs
        scores = jnp.dot(queries_c, keys_c.T, preferred_element_type=jnp.float32)
        same = (doc_c[:, None] == doc_c[None, :]) & later
        spans = running_c.T[:, :, None] - running_c.T[:, None, :]
        decay_mat = jnp.exp(jnp.where(same[None], spans, -jnp.inf))
        mixing = (scores[None] * decay_mat).astype(jnp.bfloat16)
        within = jnp.einsum('hts,shp->thp', mixing.astype(jnp.float32), scaled_c.reshape(STRETCH, HEADS, HEAD_DIM).astype(jnp.float32)).reshape(STRETCH, inner)
        readout = jnp.dot(queries_c, state_c.astype(jnp.bfloat16).T, preferred_element_type=jnp.float32)
        carry_weight = jnp.exp(jnp.where((doc_c == prev_c)[:, None], running_c - base_c[None, :], -jnp.inf))
        direct = values_c.astype(jnp.float32) * jnp.repeat(skip_gain, HEAD_DIM)[None, :]
        return within + readout * jnp.repeat(carry_weight, HEAD_DIM, axis=1) + direct
    outputs = lax.map(stretch_out, (blocked(values), blocked(scaled), blocked(input_map), blocked(output_map), blocked(running), blocked(doc_ids), base, prev_doc, state_in)).reshape(STREAM, inner)
    gated = outputs * jax.nn.silu(packed_gate.astype(jnp.float32))
    normed = gated * lax.rsqrt(lax.optimization_barrier(jnp.mean(gated * gated, axis=1, keepdims=True)) + 1e-05) * norm_gain
    mixed_out = normed.astype(jnp.bfloat16).reshape(STRETCHES, STRETCH, inner)[deal_order].reshape(STREAM, inner)

    def one_doc(document):
        last = (lax.dynamic_index_in_dim(ends, document, keepdims=False) - 1).astype(jnp.int32)
        owner = (last // STRETCH).astype(jnp.int32)
        begin = (owner * STRETCH).astype(jnp.int32)
        running_c = lax.dynamic_slice_in_dim(running, begin, STRETCH)
        doc_c = lax.dynamic_slice_in_dim(doc_ids, begin, STRETCH)
        scaled_c = lax.dynamic_slice_in_dim(scaled, begin, STRETCH)
        keys_c = lax.dynamic_slice_in_dim(input_map, begin, STRETCH)
        running_e = lax.dynamic_index_in_dim(running, last, keepdims=False)
        weight = jnp.exp(jnp.where((doc_c == document)[:, None], running_e[None, :] - running_c, -jnp.inf))
        weighted = (scaled_c.astype(jnp.float32) * jnp.repeat(weight, HEAD_DIM, axis=1)).astype(jnp.bfloat16)
        part = jnp.dot(weighted.T, keys_c, preferred_element_type=jnp.float32)
        base_c = lax.dynamic_index_in_dim(base, owner, keepdims=False)
        prev_c = lax.dynamic_index_in_dim(prev_doc, owner, keepdims=False)
        state_c = lax.dynamic_index_in_dim(state_in, owner, keepdims=False)
        carry_weight = jnp.exp(jnp.where(prev_c == document, running_e - base_c, -jnp.inf))
        return part + jnp.repeat(carry_weight, HEAD_DIM)[:, None] * state_c
    final_states = lax.map(one_doc, jnp.arange(DOCS, dtype=jnp.int32))
    return (mixed_out, final_states)
```

```python
import jax
import jax.numpy as jnp
from jax import lax
from jax.sharding import PartitionSpec as P

HEADS = 40
HEAD_DIM = 64
STATE = 128
KERNEL = 4
STRETCH = 256
INNER = 2560
CHANNELS = 2816
LEAD = KERNEL - 1
FINAL_VIA_ALL_TO_ALL = True

f32 = jnp.float32
bf16 = jnp.bfloat16


def doc_index(ends, positions):
    return jnp.sum((ends[None, :] <= positions[..., None]).astype(jnp.int32), axis=-1)


def per_head(x):
    return jnp.repeat(x, HEAD_DIM, axis=-1)


def conv_rows(ext, ext_doc, out_doc, conv_weight, conv_bias):
    rows = out_doc.shape[-1]
    accum = jnp.zeros(ext.shape[:-2] + (rows, CHANNELS), f32) + conv_bias
    for offset in range(KERNEL):
        keep = (ext_doc[..., offset : offset + rows] == out_doc).astype(f32)
        accum = (
            accum
            + conv_weight[offset]
            * ext[..., offset : offset + rows, :].astype(f32)
            * keep[..., None]
        )
    return jax.nn.silu(accum).astype(bf16)


def body(
    mixer_in,
    gate_input,
    step_raw,
    lengths,
    deal_order,
    conv_weight,
    conv_bias,
    step_bias,
    decay_rate,
    skip_gain,
    norm_gain,
):
    n = deal_order.shape[0]
    docs = lengths.shape[0]
    me = lax.axis_index("seq")
    rows_here = INNER // n
    mine = deal_order[me]
    ends = jnp.cumsum(lengths).astype(jnp.int32)
    lane = jnp.arange(STRETCH, dtype=jnp.int32)
    doc = doc_index(ends, mine * STRETCH + lane)
    end_doc_mine = doc[-1]

    step = jax.nn.softplus(step_raw.astype(f32) + step_bias)
    log_decay = -decay_rate * step
    lc = jnp.cumsum(log_decay, axis=0)
    total = lc[-1]

    ext_local = jnp.concatenate([jnp.zeros((LEAD, CHANNELS), bf16), mixer_in], 0)
    ext_doc_local = jnp.concatenate([jnp.full((LEAD,), -1, jnp.int32), doc], 0)
    mixed_local = conv_rows(ext_local, ext_doc_local, doc, conv_weight, conv_bias)
    scaled_local = (
        mixed_local[:, :INNER].astype(f32) * per_head(step)
    ).astype(bf16)
    keys_local = mixed_local[:, INNER : INNER + STATE]
    weight_end = jnp.where(
        ((doc == end_doc_mine) & (lane >= LEAD))[:, None], jnp.exp(total[None, :] - lc), 0.0
    )
    weighted_local = (scaled_local.astype(f32) * per_head(weight_end)).astype(bf16)
    state_part = jnp.dot(weighted_local.T, keys_local, preferred_element_type=f32)
    gathered_states = lax.all_gather(state_part.astype(bf16), "seq", axis=0, tiled=False)

    doc_last = ends - 1
    doc_owner = doc_last // STRETCH
    doc_at = doc_last - doc_owner * STRETCH
    lc_at_end = jnp.where(
        (doc_owner == mine)[:, None], lc[jnp.clip(doc_at, 0, STRETCH - 1)], 0.0
    )
    w_lead = jnp.where(
        (doc[:LEAD] == end_doc_mine)[:, None], jnp.exp(total[None, :] - lc[:LEAD]), 0.0
    )
    edge_rows = jnp.concatenate([mixer_in[:LEAD], mixer_in[STRETCH - LEAD :]], 0).astype(f32)
    pieces = [
        edge_rows.reshape(-1),
        total,
        step[:LEAD].reshape(-1),
        w_lead.reshape(-1),
        lc_at_end.reshape(-1),
    ]
    flat = jnp.concatenate(pieces)
    width = flat.shape[0]
    padded_width = -(-width // 128) * 128
    flat = jnp.pad(flat, (0, padded_width - width))
    small = lax.all_gather(flat, "seq", axis=0, tiled=False)

    slots = jnp.arange(n, dtype=jnp.int32)
    holder = jnp.sum(
        jnp.where(deal_order[None, :] == slots[:, None], slots[None, :], 0), axis=1
    )
    seq_small = jnp.take(small, holder, axis=0)
    cursor = 0
    sizes = [2 * LEAD * CHANNELS, HEADS, LEAD * HEADS, LEAD * HEADS, docs * HEADS]
    cut = []
    for size in sizes:
        cut.append((cursor, cursor + size))
        cursor += size
    edge_seq = seq_small[:, cut[0][0] : cut[0][1]].reshape(n, 2 * LEAD, CHANNELS)
    totals_seq = seq_small[:, cut[1][0] : cut[1][1]]
    step_lead_seq = seq_small[:, cut[2][0] : cut[2][1]].reshape(n, LEAD, HEADS)
    w_lead_seq = seq_small[:, cut[3][0] : cut[3][1]].reshape(n, LEAD, HEADS)
    lc_end = jnp.sum(small[:, cut[4][0] : cut[4][1]], axis=0).reshape(docs, HEADS)

    head_seq = edge_seq[:, :LEAD].astype(bf16)
    tail_seq = edge_seq[:, LEAD:].astype(bf16)
    prev_tail = jnp.concatenate([jnp.zeros((1, LEAD, CHANNELS), bf16), tail_seq[:-1]], 0)
    ext6 = jnp.concatenate([prev_tail, head_seq], 1)
    ext6_pos = slots[:, None] * STRETCH - LEAD + jnp.arange(2 * LEAD, dtype=jnp.int32)[None, :]
    ext6_doc = jnp.where(ext6_pos >= 0, doc_index(ends, ext6_pos), -1)
    lead_doc = ext6_doc[:, LEAD:]
    mixed_lead = conv_rows(ext6, ext6_doc, lead_doc, conv_weight, conv_bias)
    scaled_lead = (mixed_lead[..., :INNER].astype(f32) * per_head(step_lead_seq)).astype(bf16)
    keys_lead = mixed_lead[..., INNER : INNER + STATE]
    weighted_lead = (scaled_lead.astype(f32) * per_head(w_lead_seq)).astype(bf16)

    mixed = jnp.concatenate([mixed_lead[mine], mixed_local[LEAD:]], 0)
    values = mixed[:, :INNER]
    keys = mixed[:, INNER : INNER + STATE]
    queries = mixed[:, INNER + STATE :]
    scaled = (values.astype(f32) * per_head(step)).astype(bf16)

    end_doc_seq = doc_index(ends, slots * STRETCH + STRETCH - 1)
    prev_seq = jnp.where(slots > 0, doc_index(ends, slots * STRETCH - 1), -1)
    between = (slots[None, :, None] < slots[None, None, :]) & (
        slots[None, None, :] < slots[:, None, None]
    )
    gap = jnp.sum(jnp.where(between[..., None], totals_seq[None, None], 0.0), axis=2)
    allowed = (slots[None, :] < slots[:, None]) & (end_doc_seq[None, :] == prev_seq[:, None])
    cross = jnp.where(allowed[..., None], jnp.exp(gap), 0.0)
    cross_dev = jnp.take(cross, deal_order, axis=1)

    receivers = jnp.concatenate([mine[None], doc_owner])
    recv_cross = cross[receivers]
    lead_mix = (
        per_head(recv_cross)[:, :, None, :] * weighted_lead.astype(f32)[None]
    ).reshape(receivers.shape[0], n * LEAD, INNER)
    lead_state = jnp.einsum(
        "rxk,xn->rkn",
        lead_mix,
        keys_lead.reshape(n * LEAD, STATE).astype(f32),
        precision=lax.Precision.HIGHEST,
    )

    scores = jnp.dot(queries, keys.T, preferred_element_type=f32)
    later = lane[:, None] >= lane[None, :]
    same = (doc[:, None] == doc[None, :]) & later
    spans = lc.T[:, :, None] - lc.T[:, None, :]
    mixing = (scores[None] * jnp.exp(jnp.where(same[None], spans, -jnp.inf))).astype(bf16)
    within = jnp.einsum(
        "hts,shp->thp",
        mixing,
        scaled.reshape(STRETCH, HEADS, HEAD_DIM),
        preferred_element_type=f32,
    ).reshape(STRETCH, INNER)
    direct = values.astype(f32) * per_head(skip_gain)[None, :]

    doc_ids = jnp.arange(docs, dtype=jnp.int32)
    lc_own_end = lc[jnp.clip(doc_at, 0, STRETCH - 1)]
    final_weight = jnp.where(
        ((doc[None, :] == doc_ids[:, None]) & (doc_owner == mine)[:, None])[..., None],
        jnp.exp(lc_own_end[:, None, :] - lc[None]),
        0.0,
    )
    final_weighted = (scaled.astype(f32)[None] * per_head(final_weight)).astype(bf16)
    final_part = jnp.einsum(
        "dsk,sn->dkn", final_weighted, keys, preferred_element_type=f32
    ).astype(bf16)
    if FINAL_VIA_ALL_TO_ALL:
        parts_in = lax.all_to_all(
            final_part.reshape(docs, n, rows_here, STATE), "seq", 1, 1, tiled=True
        )
        part_here = jnp.sum(parts_in.astype(f32), axis=1)
    else:
        part_here = jnp.transpose(
            lax.psum_scatter(
                jnp.transpose(final_part, (1, 0, 2)), "seq", scatter_dimension=0, tiled=True
            ),
            (1, 0, 2),
        ).astype(f32)

    gs = gathered_states.astype(f32)
    state_in = (
        jnp.sum(
            cross_dev[mine][:, :, None, None]
            * gs.reshape(n, HEADS, HEAD_DIM, STATE),
            axis=0,
        ).reshape(INNER, STATE)
        + lead_state[0]
    )
    readout = jnp.dot(queries, state_in.astype(bf16).T, preferred_element_type=f32)
    carry_weight = jnp.exp(jnp.where((doc == prev_seq[mine])[:, None], lc, -jnp.inf))
    outputs = within + readout * per_head(carry_weight) + direct
    gated = outputs * jax.nn.silu(gate_input.astype(f32))
    normed = gated * lax.rsqrt(jnp.mean(gated * gated, axis=1, keepdims=True) + 1e-05) * norm_gain
    mixed_out = normed.astype(bf16)

    row_ids = me * rows_here + jnp.arange(rows_here, dtype=jnp.int32)
    row_head = row_ids // HEAD_DIM
    gs_rows = lax.dynamic_slice_in_dim(gs, me * rows_here, rows_here, axis=1)
    owner_cross = cross_dev[doc_owner][:, :, row_head]
    owner_in = jnp.einsum("dkr,krn->drn", owner_cross, gs_rows, precision=lax.Precision.HIGHEST)
    owner_in = owner_in + lax.dynamic_slice_in_dim(lead_state[1:], me * rows_here, rows_here, axis=1)
    carry_final = jnp.where(
        (prev_seq[doc_owner] == doc_ids)[:, None], jnp.exp(lc_end[:, row_head]), 0.0
    )
    final_states = part_here + carry_final[..., None] * owner_in
    return (mixed_out, final_states)


def solution(mesh):
    return jax.shard_map(
        body,
        mesh=mesh,
        in_specs=(
            P(("dp", "seq"), None),
            P(("dp", "seq"), None),
            P(("dp", "seq"), None),
            P("dp"),
            P("dp"),
            P(),
            P(),
            P(),
            P(),
            P(),
            P(),
        ),
        out_specs=(P(("dp", "seq"), None), P("dp", "seq", None)),
        check_vma=False,
    )
```

```python
import jax
import jax.numpy as jnp
from jax import lax
from jax.sharding import PartitionSpec as P

HEADS = 40
HEAD_DIM = 64
STATE = 128
KERNEL = 4
STRETCH = 256
INNER = 2560
CHANNELS = 2816
LEAD = KERNEL - 1
FINAL_VIA_ALL_TO_ALL = True

f32 = jnp.float32
bf16 = jnp.bfloat16


def doc_index(ends, positions):
    return jnp.sum((ends[None, :] <= positions[..., None]).astype(jnp.int32), axis=-1)


def per_head(x):
    expand = (
        jnp.arange(HEADS * HEAD_DIM, dtype=jnp.int32)[None, :] // HEAD_DIM
        == jnp.arange(HEADS, dtype=jnp.int32)[:, None]
    ).astype(f32)
    return jnp.matmul(x, expand, precision=lax.Precision.HIGHEST)


def conv_rows(ext, ext_doc, out_doc, conv_weight, conv_bias):
    rows = out_doc.shape[-1]
    accum = jnp.zeros(ext.shape[:-2] + (rows, CHANNELS), f32) + conv_bias
    for offset in range(KERNEL):
        keep = (ext_doc[..., offset : offset + rows] == out_doc).astype(f32)
        accum = (
            accum
            + conv_weight[offset]
            * ext[..., offset : offset + rows, :].astype(f32)
            * keep[..., None]
        )
    return jax.nn.silu(accum).astype(bf16)


def body(
    mixer_in,
    gate_input,
    step_raw,
    lengths,
    deal_order,
    conv_weight,
    conv_bias,
    step_bias,
    decay_rate,
    skip_gain,
    norm_gain,
):
    n = deal_order.shape[0]
    docs = lengths.shape[0]
    me = lax.axis_index("seq")
    rows_here = INNER // n
    mine = deal_order[me]
    ends = jnp.cumsum(lengths).astype(jnp.int32)
    lane = jnp.arange(STRETCH, dtype=jnp.int32)
    doc = doc_index(ends, mine * STRETCH + lane)
    end_doc_mine = doc[-1]

    step = jax.nn.softplus(step_raw.astype(f32) + step_bias)
    log_decay = -decay_rate * step
    lc = jnp.cumsum(log_decay, axis=0)
    total = lc[-1]

    ext_local = jnp.concatenate([jnp.zeros((LEAD, CHANNELS), bf16), mixer_in], 0)
    ext_doc_local = jnp.concatenate([jnp.full((LEAD,), -1, jnp.int32), doc], 0)
    mixed_local = conv_rows(ext_local, ext_doc_local, doc, conv_weight, conv_bias)
    scaled_local = (
        mixed_local[:, :INNER].astype(f32) * per_head(step)
    ).astype(bf16)
    keys_local = mixed_local[:, INNER : INNER + STATE]
    weight_end = jnp.where(
        ((doc == end_doc_mine) & (lane >= LEAD))[:, None], jnp.exp(total[None, :] - lc), 0.0
    )
    weighted_local = (scaled_local.astype(f32) * per_head(weight_end)).astype(bf16)
    state_part = jnp.dot(weighted_local.T, keys_local, preferred_element_type=f32)
    gathered_states = lax.all_gather(state_part.astype(bf16), "seq", axis=0, tiled=False)

    doc_last = ends - 1
    doc_owner = doc_last // STRETCH
    doc_at = doc_last - doc_owner * STRETCH
    lc_at_end = jnp.where(
        (doc_owner == mine)[:, None], lc[jnp.clip(doc_at, 0, STRETCH - 1)], 0.0
    )
    w_lead = jnp.where(
        (doc[:LEAD] == end_doc_mine)[:, None], jnp.exp(total[None, :] - lc[:LEAD]), 0.0
    )
    edge_rows = jnp.concatenate([mixer_in[:LEAD], mixer_in[STRETCH - LEAD :]], 0).astype(f32)
    pieces = [
        edge_rows.reshape(-1),
        total,
        step[:LEAD].reshape(-1),
        w_lead.reshape(-1),
        lc_at_end.reshape(-1),
    ]
    flat = jnp.concatenate(pieces)
    width = flat.shape[0]
    padded_width = -(-width // 128) * 128
    flat = jnp.pad(flat, (0, padded_width - width))
    small = lax.all_to_all(
        jnp.broadcast_to(flat[None], (n, padded_width)), "seq", 0, 0, tiled=True
    )

    slots = jnp.arange(n, dtype=jnp.int32)
    holder = jnp.sum(
        jnp.where(deal_order[None, :] == slots[:, None], slots[None, :], 0), axis=1
    )
    seq_small = jnp.take(small, holder, axis=0)
    cursor = 0
    sizes = [2 * LEAD * CHANNELS, HEADS, LEAD * HEADS, LEAD * HEADS, docs * HEADS]
    cut = []
    for size in sizes:
        cut.append((cursor, cursor + size))
        cursor += size
    edge_seq = seq_small[:, cut[0][0] : cut[0][1]].reshape(n, 2 * LEAD, CHANNELS)
    totals_seq = seq_small[:, cut[1][0] : cut[1][1]]
    step_lead_seq = seq_small[:, cut[2][0] : cut[2][1]].reshape(n, LEAD, HEADS)
    w_lead_seq = seq_small[:, cut[3][0] : cut[3][1]].reshape(n, LEAD, HEADS)
    lc_end = jnp.sum(small[:, cut[4][0] : cut[4][1]], axis=0).reshape(docs, HEADS)

    head_seq = edge_seq[:, :LEAD].astype(bf16)
    tail_seq = edge_seq[:, LEAD:].astype(bf16)
    prev_tail = jnp.concatenate([jnp.zeros((1, LEAD, CHANNELS), bf16), tail_seq[:-1]], 0)
    ext6 = jnp.concatenate([prev_tail, head_seq], 1)
    ext6_pos = slots[:, None] * STRETCH - LEAD + jnp.arange(2 * LEAD, dtype=jnp.int32)[None, :]
    ext6_doc = jnp.where(ext6_pos >= 0, doc_index(ends, ext6_pos), -1)
    lead_doc = ext6_doc[:, LEAD:]
    mixed_lead = conv_rows(ext6, ext6_doc, lead_doc, conv_weight, conv_bias)
    scaled_lead = (mixed_lead[..., :INNER].astype(f32) * per_head(step_lead_seq)).astype(bf16)
    keys_lead = mixed_lead[..., INNER : INNER + STATE]
    weighted_lead = (scaled_lead.astype(f32) * per_head(w_lead_seq)).astype(bf16)

    mixed = jnp.concatenate([mixed_lead[mine], mixed_local[LEAD:]], 0)
    values = mixed[:, :INNER]
    keys = mixed[:, INNER : INNER + STATE]
    queries = mixed[:, INNER + STATE :]
    scaled = (values.astype(f32) * per_head(step)).astype(bf16)

    end_doc_seq = doc_index(ends, slots * STRETCH + STRETCH - 1)
    prev_seq = jnp.where(slots > 0, doc_index(ends, slots * STRETCH - 1), -1)
    between = (slots[None, :, None] < slots[None, None, :]) & (
        slots[None, None, :] < slots[:, None, None]
    )
    gap = jnp.sum(jnp.where(between[..., None], totals_seq[None, None], 0.0), axis=2)
    allowed = (slots[None, :] < slots[:, None]) & (end_doc_seq[None, :] == prev_seq[:, None])
    cross = jnp.where(allowed[..., None], jnp.exp(gap), 0.0)
    cross_dev = jnp.take(cross, deal_order, axis=1)

    receivers = jnp.concatenate([mine[None], doc_owner])
    recv_cross = cross[receivers]
    lead_mix = (
        per_head(recv_cross)[:, :, None, :] * weighted_lead.astype(f32)[None]
    ).reshape(receivers.shape[0], n * LEAD, INNER)
    lead_state = jnp.einsum(
        "rxk,xn->rkn",
        lead_mix,
        keys_lead.reshape(n * LEAD, STATE).astype(f32),
        precision=lax.Precision.HIGHEST,
    )

    scores = jnp.dot(queries, keys.T, preferred_element_type=f32)
    later = lane[:, None] >= lane[None, :]
    same = (doc[:, None] == doc[None, :]) & later
    spans = lc.T[:, :, None] - lc.T[:, None, :]
    mixing = (scores[None] * jnp.exp(jnp.where(same[None], spans, -jnp.inf))).astype(bf16)
    within = jnp.einsum(
        "hts,shp->thp",
        mixing,
        scaled.reshape(STRETCH, HEADS, HEAD_DIM),
        preferred_element_type=f32,
    ).reshape(STRETCH, INNER)
    direct = values.astype(f32) * per_head(skip_gain)[None, :]

    doc_ids = jnp.arange(docs, dtype=jnp.int32)
    lc_own_end = lc[jnp.clip(doc_at, 0, STRETCH - 1)]
    final_weight = jnp.where(
        ((doc[None, :] == doc_ids[:, None]) & (doc_owner == mine)[:, None])[..., None],
        jnp.exp(lc_own_end[:, None, :] - lc[None]),
        0.0,
    )
    final_weighted = (scaled.astype(f32)[None] * per_head(final_weight)).astype(bf16)
    final_part = jnp.einsum(
        "dsk,sn->dkn", final_weighted, keys, preferred_element_type=f32
    ).astype(bf16)
    if FINAL_VIA_ALL_TO_ALL:
        parts_in = lax.all_to_all(
            final_part.reshape(docs, n, rows_here, STATE), "seq", 1, 1, tiled=True
        )
        part_here = jnp.sum(parts_in.astype(f32), axis=1)
    else:
        part_here = jnp.transpose(
            lax.psum_scatter(
                jnp.transpose(final_part, (1, 0, 2)), "seq", scatter_dimension=0, tiled=True
            ),
            (1, 0, 2),
        ).astype(f32)

    own_cross = cross_dev[mine]
    state_in = lead_state[0].reshape(HEADS, HEAD_DIM, STATE)
    for k in range(n):
        state_in = state_in + own_cross[k][:, None, None] * gathered_states[k].astype(
            f32
        ).reshape(HEADS, HEAD_DIM, STATE)
    state_in = state_in.reshape(INNER, STATE)
    readout = jnp.dot(queries, state_in.astype(bf16).T, preferred_element_type=f32)
    carry_weight = jnp.exp(jnp.where((doc == prev_seq[mine])[:, None], lc, -jnp.inf))
    outputs = within + readout * per_head(carry_weight) + direct
    gated = outputs * jax.nn.silu(gate_input.astype(f32))
    normed = gated * lax.rsqrt(jnp.mean(gated * gated, axis=1, keepdims=True) + 1e-05) * norm_gain
    mixed_out = normed.astype(bf16)

    row_ids = me * rows_here + jnp.arange(rows_here, dtype=jnp.int32)
    row_head = row_ids // HEAD_DIM
    gs_rows = lax.dynamic_slice_in_dim(
        gathered_states, me * rows_here, rows_here, axis=1
    ).astype(f32)
    owner_cross = cross_dev[doc_owner][:, :, row_head]
    owner_in = jnp.einsum("dkr,krn->drn", owner_cross, gs_rows, precision=lax.Precision.HIGHEST)
    owner_in = owner_in + lax.dynamic_slice_in_dim(lead_state[1:], me * rows_here, rows_here, axis=1)
    carry_final = jnp.where(
        (prev_seq[doc_owner] == doc_ids)[:, None], jnp.exp(lc_end[:, row_head]), 0.0
    )
    final_states = part_here + carry_final[..., None] * owner_in
    return (mixed_out, final_states)


def solution(mesh):
    return jax.shard_map(
        body,
        mesh=mesh,
        in_specs=(
            P(("dp", "seq"), None),
            P(("dp", "seq"), None),
            P(("dp", "seq"), None),
            P("dp"),
            P("dp"),
            P(),
            P(),
            P(),
            P(),
            P(),
            P(),
        ),
        out_specs=(P(("dp", "seq"), None), P("dp", "seq", None)),
        check_vma=False,
    )
```

```python
import jax
import jax.numpy as jnp
from jax import lax
from jax.sharding import PartitionSpec as P

HEADS = 40
HEAD_DIM = 64
STATE = 128
KERNEL = 4
STRETCH = 256
INNER = 2560
CHANNELS = 2816
LEAD = KERNEL - 1
FINAL_VIA_ALL_TO_ALL = True

f32 = jnp.float32
bf16 = jnp.bfloat16


def doc_index(ends, positions):
    return jnp.sum((ends[None, :] <= positions[..., None]).astype(jnp.int32), axis=-1)


def per_head(x):
    expand = (
        jnp.arange(HEADS * HEAD_DIM, dtype=jnp.int32)[None, :] // HEAD_DIM
        == jnp.arange(HEADS, dtype=jnp.int32)[:, None]
    ).astype(f32)
    return jnp.matmul(x, expand, precision=lax.Precision.HIGHEST)


def conv_rows(ext, ext_doc, out_doc, conv_weight, conv_bias):
    rows = out_doc.shape[-1]
    accum = jnp.zeros(ext.shape[:-2] + (rows, CHANNELS), f32) + conv_bias
    for offset in range(KERNEL):
        keep = (ext_doc[..., offset : offset + rows] == out_doc).astype(f32)
        accum = (
            accum
            + conv_weight[offset]
            * ext[..., offset : offset + rows, :].astype(f32)
            * keep[..., None]
        )
    return jax.nn.silu(accum).astype(bf16)


def body(
    mixer_in,
    gate_input,
    step_raw,
    lengths,
    deal_order,
    conv_weight,
    conv_bias,
    step_bias,
    decay_rate,
    skip_gain,
    norm_gain,
):
    n = deal_order.shape[0]
    docs = lengths.shape[0]
    me = lax.axis_index("seq")
    rows_here = INNER // n
    mine = deal_order[me]
    ends = jnp.cumsum(lengths).astype(jnp.int32)
    lane = jnp.arange(STRETCH, dtype=jnp.int32)
    doc = doc_index(ends, mine * STRETCH + lane)
    end_doc_mine = doc[-1]

    step = jax.nn.softplus(step_raw.astype(f32) + step_bias)
    log_decay = -decay_rate * step
    lc = jnp.cumsum(log_decay, axis=0)
    total = lc[-1]

    ext_local = jnp.concatenate([jnp.zeros((LEAD, CHANNELS), bf16), mixer_in], 0)
    ext_doc_local = jnp.concatenate([jnp.full((LEAD,), -1, jnp.int32), doc], 0)
    mixed_local = conv_rows(ext_local, ext_doc_local, doc, conv_weight, conv_bias)
    scaled_local = (
        mixed_local[:, :INNER].astype(f32) * per_head(step)
    ).astype(bf16)
    keys_local = mixed_local[:, INNER : INNER + STATE]
    weight_end = jnp.where(
        ((doc == end_doc_mine) & (lane >= LEAD))[:, None], jnp.exp(total[None, :] - lc), 0.0
    )
    weighted_local = (scaled_local.astype(f32) * per_head(weight_end)).astype(bf16)
    state_part = jnp.dot(weighted_local.T, keys_local, preferred_element_type=f32)

    doc_last = ends - 1
    doc_owner = doc_last // STRETCH
    doc_at = doc_last - doc_owner * STRETCH
    lc_at_end = jnp.where(
        (doc_owner == mine)[:, None], lc[jnp.clip(doc_at, 0, STRETCH - 1)], 0.0
    )
    w_lead = jnp.where(
        (doc[:LEAD] == end_doc_mine)[:, None], jnp.exp(total[None, :] - lc[:LEAD]), 0.0
    )
    edge_rows = jnp.concatenate([mixer_in[:LEAD], mixer_in[STRETCH - LEAD :]], 0).astype(f32)
    pieces = [
        edge_rows.reshape(-1),
        total,
        step[:LEAD].reshape(-1),
        w_lead.reshape(-1),
        lc_at_end.reshape(-1),
    ]
    flat = jnp.concatenate(pieces)
    width = flat.shape[0]
    padded_width = -(-width // 128) * 128
    flat = jnp.pad(flat, (0, padded_width - width))
    flat, state_send = lax.optimization_barrier((flat, state_part.astype(bf16)))
    gathered_states = lax.all_gather(state_send, "seq", axis=0, tiled=False)
    small = lax.all_to_all(
        jnp.broadcast_to(flat[None], (n, padded_width)), "seq", 0, 0, tiled=True
    )

    slots = jnp.arange(n, dtype=jnp.int32)
    holder = jnp.sum(
        jnp.where(deal_order[None, :] == slots[:, None], slots[None, :], 0), axis=1
    )
    seq_small = jnp.take(small, holder, axis=0)
    cursor = 0
    sizes = [2 * LEAD * CHANNELS, HEADS, LEAD * HEADS, LEAD * HEADS, docs * HEADS]
    cut = []
    for size in sizes:
        cut.append((cursor, cursor + size))
        cursor += size
    edge_seq = seq_small[:, cut[0][0] : cut[0][1]].reshape(n, 2 * LEAD, CHANNELS)
    totals_seq = seq_small[:, cut[1][0] : cut[1][1]]
    step_lead_seq = seq_small[:, cut[2][0] : cut[2][1]].reshape(n, LEAD, HEADS)
    w_lead_seq = seq_small[:, cut[3][0] : cut[3][1]].reshape(n, LEAD, HEADS)
    lc_end = jnp.sum(small[:, cut[4][0] : cut[4][1]], axis=0).reshape(docs, HEADS)

    head_seq = edge_seq[:, :LEAD].astype(bf16)
    tail_seq = edge_seq[:, LEAD:].astype(bf16)
    prev_tail = jnp.concatenate([jnp.zeros((1, LEAD, CHANNELS), bf16), tail_seq[:-1]], 0)
    ext6 = jnp.concatenate([prev_tail, head_seq], 1)
    ext6_pos = slots[:, None] * STRETCH - LEAD + jnp.arange(2 * LEAD, dtype=jnp.int32)[None, :]
    ext6_doc = jnp.where(ext6_pos >= 0, doc_index(ends, ext6_pos), -1)
    lead_doc = ext6_doc[:, LEAD:]
    mixed_lead = conv_rows(ext6, ext6_doc, lead_doc, conv_weight, conv_bias)
    scaled_lead = (mixed_lead[..., :INNER].astype(f32) * per_head(step_lead_seq)).astype(bf16)
    keys_lead = mixed_lead[..., INNER : INNER + STATE]
    weighted_lead = (scaled_lead.astype(f32) * per_head(w_lead_seq)).astype(bf16)

    mixed = jnp.concatenate([mixed_lead[mine], mixed_local[LEAD:]], 0)
    values = mixed[:, :INNER]
    keys = mixed[:, INNER : INNER + STATE]
    queries = mixed[:, INNER + STATE :]
    scaled = (values.astype(f32) * per_head(step)).astype(bf16)

    end_doc_seq = doc_index(ends, slots * STRETCH + STRETCH - 1)
    prev_seq = jnp.where(slots > 0, doc_index(ends, slots * STRETCH - 1), -1)
    between = (slots[None, :, None] < slots[None, None, :]) & (
        slots[None, None, :] < slots[:, None, None]
    )
    gap = jnp.sum(jnp.where(between[..., None], totals_seq[None, None], 0.0), axis=2)
    allowed = (slots[None, :] < slots[:, None]) & (end_doc_seq[None, :] == prev_seq[:, None])
    cross = jnp.where(allowed[..., None], jnp.exp(gap), 0.0)
    cross_dev = jnp.take(cross, deal_order, axis=1)

    receivers = jnp.concatenate([mine[None], doc_owner])
    recv_cross = cross[receivers]
    lead_mix = (
        per_head(recv_cross)[:, :, None, :] * weighted_lead.astype(f32)[None]
    ).reshape(receivers.shape[0], n * LEAD, INNER)
    lead_state = jnp.einsum(
        "rxk,xn->rkn",
        lead_mix,
        keys_lead.reshape(n * LEAD, STATE).astype(f32),
        precision=lax.Precision.HIGHEST,
    )

    scores = jnp.dot(queries, keys.T, preferred_element_type=f32)
    later = lane[:, None] >= lane[None, :]
    same = (doc[:, None] == doc[None, :]) & later
    spans = lc.T[:, :, None] - lc.T[:, None, :]
    mixing = (scores[None] * jnp.exp(jnp.where(same[None], spans, -jnp.inf))).astype(bf16)
    within = jnp.einsum(
        "hts,shp->thp",
        mixing,
        scaled.reshape(STRETCH, HEADS, HEAD_DIM),
        preferred_element_type=f32,
    ).reshape(STRETCH, INNER)
    direct = values.astype(f32) * per_head(skip_gain)[None, :]

    doc_ids = jnp.arange(docs, dtype=jnp.int32)
    lc_own_end = lc[jnp.clip(doc_at, 0, STRETCH - 1)]
    final_weight = jnp.where(
        ((doc[None, :] == doc_ids[:, None]) & (doc_owner == mine)[:, None])[..., None],
        jnp.exp(lc_own_end[:, None, :] - lc[None]),
        0.0,
    )
    final_weighted = (scaled.astype(f32)[None] * per_head(final_weight)).astype(bf16)
    final_part = jnp.einsum(
        "dsk,sn->dkn", final_weighted, keys, preferred_element_type=f32
    ).astype(bf16)
    if FINAL_VIA_ALL_TO_ALL:
        parts_in = lax.all_to_all(
            final_part.reshape(docs, n, rows_here, STATE), "seq", 1, 1, tiled=True
        )
        part_here = jnp.sum(parts_in.astype(f32), axis=1)
    else:
        part_here = jnp.transpose(
            lax.psum_scatter(
                jnp.transpose(final_part, (1, 0, 2)), "seq", scatter_dimension=0, tiled=True
            ),
            (1, 0, 2),
        ).astype(f32)

    own_cross = cross_dev[mine]
    state_in = lead_state[0].reshape(HEADS, HEAD_DIM, STATE)
    for k in range(n):
        state_in = state_in + own_cross[k][:, None, None] * gathered_states[k].astype(
            f32
        ).reshape(HEADS, HEAD_DIM, STATE)
    state_in = state_in.reshape(INNER, STATE)
    readout = jnp.dot(queries, state_in.astype(bf16).T, preferred_element_type=f32)
    carry_weight = jnp.exp(jnp.where((doc == prev_seq[mine])[:, None], lc, -jnp.inf))
    outputs = within + readout * per_head(carry_weight) + direct
    gated = outputs * jax.nn.silu(gate_input.astype(f32))
    normed = gated * lax.rsqrt(jnp.mean(gated * gated, axis=1, keepdims=True) + 1e-05) * norm_gain
    mixed_out = normed.astype(bf16)

    row_ids = me * rows_here + jnp.arange(rows_here, dtype=jnp.int32)
    row_head = row_ids // HEAD_DIM
    gs_rows = lax.dynamic_slice_in_dim(
        gathered_states, me * rows_here, rows_here, axis=1
    ).astype(f32)
    owner_cross = cross_dev[doc_owner][:, :, row_head]
    owner_in = jnp.einsum("dkr,krn->drn", owner_cross, gs_rows, precision=lax.Precision.HIGHEST)
    owner_in = owner_in + lax.dynamic_slice_in_dim(lead_state[1:], me * rows_here, rows_here, axis=1)
    carry_final = jnp.where(
        (prev_seq[doc_owner] == doc_ids)[:, None], jnp.exp(lc_end[:, row_head]), 0.0
    )
    final_states = part_here + carry_final[..., None] * owner_in
    return (mixed_out, final_states)


def solution(mesh):
    return jax.shard_map(
        body,
        mesh=mesh,
        in_specs=(
            P(("dp", "seq"), None),
            P(("dp", "seq"), None),
            P(("dp", "seq"), None),
            P("dp"),
            P("dp"),
            P(),
            P(),
            P(),
            P(),
            P(),
            P(),
        ),
        out_specs=(P(("dp", "seq"), None), P("dp", "seq", None)),
        check_vma=False,
    )
```

```python
import jax
import jax.numpy as jnp
from jax import lax
from jax.sharding import PartitionSpec as P

HEADS = 40
HEAD_DIM = 64
STATE = 128
KERNEL = 4
STRETCH = 256
INNER = 2560
CHANNELS = 2816
LEAD = KERNEL - 1
FINAL_VIA_ALL_TO_ALL = True
HEADS_ON_GATHER = 25

f32 = jnp.float32
bf16 = jnp.bfloat16


def doc_index(ends, positions):
    return jnp.sum((ends[None, :] <= positions[..., None]).astype(jnp.int32), axis=-1)


def per_head(x):
    expand = (
        jnp.arange(HEADS * HEAD_DIM, dtype=jnp.int32)[None, :] // HEAD_DIM
        == jnp.arange(HEADS, dtype=jnp.int32)[:, None]
    ).astype(f32)
    return jnp.matmul(x, expand, precision=lax.Precision.HIGHEST)


def conv_rows(ext, ext_doc, out_doc, conv_weight, conv_bias):
    rows = out_doc.shape[-1]
    accum = jnp.zeros(ext.shape[:-2] + (rows, CHANNELS), f32) + conv_bias
    for offset in range(KERNEL):
        keep = (ext_doc[..., offset : offset + rows] == out_doc).astype(f32)
        accum = (
            accum
            + conv_weight[offset]
            * ext[..., offset : offset + rows, :].astype(f32)
            * keep[..., None]
        )
    return jax.nn.silu(accum).astype(bf16)


def body(
    mixer_in,
    gate_input,
    step_raw,
    lengths,
    deal_order,
    conv_weight,
    conv_bias,
    step_bias,
    decay_rate,
    skip_gain,
    norm_gain,
):
    n = deal_order.shape[0]
    docs = lengths.shape[0]
    me = lax.axis_index("seq")
    rows_here = INNER // n
    mine = deal_order[me]
    ends = jnp.cumsum(lengths).astype(jnp.int32)
    lane = jnp.arange(STRETCH, dtype=jnp.int32)
    doc = doc_index(ends, mine * STRETCH + lane)
    end_doc_mine = doc[-1]

    step = jax.nn.softplus(step_raw.astype(f32) + step_bias)
    log_decay = -decay_rate * step
    lc = jnp.cumsum(log_decay, axis=0)
    total = lc[-1]

    ext_local = jnp.concatenate([jnp.zeros((LEAD, CHANNELS), bf16), mixer_in], 0)
    ext_doc_local = jnp.concatenate([jnp.full((LEAD,), -1, jnp.int32), doc], 0)
    mixed_local = conv_rows(ext_local, ext_doc_local, doc, conv_weight, conv_bias)
    scaled_local = (
        mixed_local[:, :INNER].astype(f32) * per_head(step)
    ).astype(bf16)
    keys_local = mixed_local[:, INNER : INNER + STATE]
    weight_end = jnp.where(
        ((doc == end_doc_mine) & (lane >= LEAD))[:, None], jnp.exp(total[None, :] - lc), 0.0
    )
    weighted_local = (scaled_local.astype(f32) * per_head(weight_end)).astype(bf16)
    state_part = jnp.dot(weighted_local.T, keys_local, preferred_element_type=f32)

    doc_last = ends - 1
    doc_owner = doc_last // STRETCH
    doc_at = doc_last - doc_owner * STRETCH
    lc_at_end = jnp.where(
        (doc_owner == mine)[:, None], lc[jnp.clip(doc_at, 0, STRETCH - 1)], 0.0
    )
    w_lead = jnp.where(
        (doc[:LEAD] == end_doc_mine)[:, None], jnp.exp(total[None, :] - lc[:LEAD]), 0.0
    )
    edge_rows = jnp.concatenate([mixer_in[:LEAD], mixer_in[STRETCH - LEAD :]], 0).astype(f32)
    pieces = [
        edge_rows.reshape(-1),
        total,
        step[:LEAD].reshape(-1),
        w_lead.reshape(-1),
        lc_at_end.reshape(-1),
    ]
    flat = jnp.concatenate(pieces)
    width = flat.shape[0]
    padded_width = -(-width // 128) * 128
    flat = jnp.pad(flat, (0, padded_width - width))
    split = HEADS_ON_GATHER * HEAD_DIM
    state_bf = state_part.astype(bf16)
    flat, send_a, send_b = lax.optimization_barrier((flat, state_bf[:split], state_bf[split:]))
    gathered_a = lax.all_gather(send_a, "seq", axis=0, tiled=False)
    gathered_b = lax.all_to_all(
        jnp.broadcast_to(send_b[None], (n,) + send_b.shape), "seq", 0, 0, tiled=True
    )
    small = lax.all_to_all(
        jnp.broadcast_to(flat[None], (n, padded_width)), "seq", 0, 0, tiled=True
    )

    slots = jnp.arange(n, dtype=jnp.int32)
    holder = jnp.sum(
        jnp.where(deal_order[None, :] == slots[:, None], slots[None, :], 0), axis=1
    )
    seq_small = jnp.take(small, holder, axis=0)
    cursor = 0
    sizes = [2 * LEAD * CHANNELS, HEADS, LEAD * HEADS, LEAD * HEADS, docs * HEADS]
    cut = []
    for size in sizes:
        cut.append((cursor, cursor + size))
        cursor += size
    edge_seq = seq_small[:, cut[0][0] : cut[0][1]].reshape(n, 2 * LEAD, CHANNELS)
    totals_seq = seq_small[:, cut[1][0] : cut[1][1]]
    step_lead_seq = seq_small[:, cut[2][0] : cut[2][1]].reshape(n, LEAD, HEADS)
    w_lead_seq = seq_small[:, cut[3][0] : cut[3][1]].reshape(n, LEAD, HEADS)
    lc_end = jnp.sum(small[:, cut[4][0] : cut[4][1]], axis=0).reshape(docs, HEADS)

    head_seq = edge_seq[:, :LEAD].astype(bf16)
    tail_seq = edge_seq[:, LEAD:].astype(bf16)
    prev_tail = jnp.concatenate([jnp.zeros((1, LEAD, CHANNELS), bf16), tail_seq[:-1]], 0)
    ext6 = jnp.concatenate([prev_tail, head_seq], 1)
    ext6_pos = slots[:, None] * STRETCH - LEAD + jnp.arange(2 * LEAD, dtype=jnp.int32)[None, :]
    ext6_doc = jnp.where(ext6_pos >= 0, doc_index(ends, ext6_pos), -1)
    lead_doc = ext6_doc[:, LEAD:]
    mixed_lead = conv_rows(ext6, ext6_doc, lead_doc, conv_weight, conv_bias)
    scaled_lead = (mixed_lead[..., :INNER].astype(f32) * per_head(step_lead_seq)).astype(bf16)
    keys_lead = mixed_lead[..., INNER : INNER + STATE]
    weighted_lead = (scaled_lead.astype(f32) * per_head(w_lead_seq)).astype(bf16)

    mixed = jnp.concatenate([mixed_lead[mine], mixed_local[LEAD:]], 0)
    values = mixed[:, :INNER]
    keys = mixed[:, INNER : INNER + STATE]
    queries = mixed[:, INNER + STATE :]
    scaled = (values.astype(f32) * per_head(step)).astype(bf16)

    end_doc_seq = doc_index(ends, slots * STRETCH + STRETCH - 1)
    prev_seq = jnp.where(slots > 0, doc_index(ends, slots * STRETCH - 1), -1)
    between = (slots[None, :, None] < slots[None, None, :]) & (
        slots[None, None, :] < slots[:, None, None]
    )
    gap = jnp.sum(jnp.where(between[..., None], totals_seq[None, None], 0.0), axis=2)
    allowed = (slots[None, :] < slots[:, None]) & (end_doc_seq[None, :] == prev_seq[:, None])
    cross = jnp.where(allowed[..., None], jnp.exp(gap), 0.0)
    cross_dev = jnp.take(cross, deal_order, axis=1)

    receivers = jnp.concatenate([mine[None], doc_owner])
    recv_cross = cross[receivers]
    lead_mix = (
        per_head(recv_cross)[:, :, None, :] * weighted_lead.astype(f32)[None]
    ).reshape(receivers.shape[0], n * LEAD, INNER)
    lead_state = jnp.einsum(
        "rxk,xn->rkn",
        lead_mix,
        keys_lead.reshape(n * LEAD, STATE).astype(f32),
        precision=lax.Precision.HIGHEST,
    )

    scores = jnp.dot(queries, keys.T, preferred_element_type=f32)
    later = lane[:, None] >= lane[None, :]
    same = (doc[:, None] == doc[None, :]) & later
    spans = lc.T[:, :, None] - lc.T[:, None, :]
    mixing = (scores[None] * jnp.exp(jnp.where(same[None], spans, -jnp.inf))).astype(bf16)
    within = jnp.einsum(
        "hts,shp->thp",
        mixing,
        scaled.reshape(STRETCH, HEADS, HEAD_DIM),
        preferred_element_type=f32,
    ).reshape(STRETCH, INNER)
    direct = values.astype(f32) * per_head(skip_gain)[None, :]

    doc_ids = jnp.arange(docs, dtype=jnp.int32)
    lc_own_end = lc[jnp.clip(doc_at, 0, STRETCH - 1)]
    final_weight = jnp.where(
        ((doc[None, :] == doc_ids[:, None]) & (doc_owner == mine)[:, None])[..., None],
        jnp.exp(lc_own_end[:, None, :] - lc[None]),
        0.0,
    )
    final_weighted = (scaled.astype(f32)[None] * per_head(final_weight)).astype(bf16)
    final_part = jnp.einsum(
        "dsk,sn->dkn", final_weighted, keys, preferred_element_type=f32
    ).astype(bf16)
    final_part, gathered_b = lax.optimization_barrier((final_part, gathered_b))
    if FINAL_VIA_ALL_TO_ALL:
        parts_in = lax.all_to_all(
            final_part.reshape(docs, n, rows_here, STATE), "seq", 1, 1, tiled=True
        )
        part_here = jnp.sum(parts_in.astype(f32), axis=1)
    else:
        part_here = jnp.transpose(
            lax.psum_scatter(
                jnp.transpose(final_part, (1, 0, 2)), "seq", scatter_dimension=0, tiled=True
            ),
            (1, 0, 2),
        ).astype(f32)

    own_w = per_head(cross_dev[mine])
    state_a = lead_state[0][:split]
    state_b = lead_state[0][split:]
    for k in range(n):
        state_a = state_a + own_w[k, :split][:, None] * gathered_a[k].astype(f32)
        state_b = state_b + own_w[k, split:][:, None] * gathered_b[k].astype(f32)
    state_in = jnp.concatenate([state_a, state_b], 0)
    readout = jnp.dot(queries, state_in.astype(bf16).T, preferred_element_type=f32)
    carry_weight = jnp.exp(jnp.where((doc == prev_seq[mine])[:, None], lc, -jnp.inf))
    outputs = within + readout * per_head(carry_weight) + direct
    gated = outputs * jax.nn.silu(gate_input.astype(f32))
    normed = gated * lax.rsqrt(jnp.mean(gated * gated, axis=1, keepdims=True) + 1e-05) * norm_gain
    mixed_out = normed.astype(bf16)

    row_ids = me * rows_here + jnp.arange(rows_here, dtype=jnp.int32)
    row_head = row_ids // HEAD_DIM
    first_row = me * rows_here
    rows_a = lax.dynamic_slice_in_dim(
        gathered_a, jnp.clip(first_row, 0, split - rows_here), rows_here, axis=1
    )
    rows_b = lax.dynamic_slice_in_dim(
        gathered_b, jnp.clip(first_row - split, 0, INNER - split - rows_here), rows_here, axis=1
    )
    gs_rows = jnp.where(first_row < split, rows_a, rows_b).astype(f32)
    owner_cross = cross_dev[doc_owner][:, :, row_head]
    owner_in = jnp.einsum("dkr,krn->drn", owner_cross, gs_rows, precision=lax.Precision.HIGHEST)
    owner_in = owner_in + lax.dynamic_slice_in_dim(lead_state[1:], me * rows_here, rows_here, axis=1)
    carry_final = jnp.where(
        (prev_seq[doc_owner] == doc_ids)[:, None], jnp.exp(lc_end[:, row_head]), 0.0
    )
    final_states = part_here + carry_final[..., None] * owner_in
    return (mixed_out, final_states)


def solution(mesh):
    return jax.shard_map(
        body,
        mesh=mesh,
        in_specs=(
            P(("dp", "seq"), None),
            P(("dp", "seq"), None),
            P(("dp", "seq"), None),
            P("dp"),
            P("dp"),
            P(),
            P(),
            P(),
            P(),
            P(),
            P(),
        ),
        out_specs=(P(("dp", "seq"), None), P("dp", "seq", None)),
        check_vma=False,
    )
```

```python
import jax
import jax.numpy as jnp
from jax import lax
from jax.sharding import PartitionSpec as P

HEADS = 40
HEAD_DIM = 64
STATE = 128
KERNEL = 4
STRETCH = 256
INNER = 2560
CHANNELS = 2816
LEAD = KERNEL - 1
FINAL_VIA_ALL_TO_ALL = True

f32 = jnp.float32
bf16 = jnp.bfloat16


def doc_index(ends, positions):
    return jnp.sum((ends[None, :] <= positions[..., None]).astype(jnp.int32), axis=-1)


def per_head(x):
    expand = (
        jnp.arange(HEADS * HEAD_DIM, dtype=jnp.int32)[None, :] // HEAD_DIM
        == jnp.arange(HEADS, dtype=jnp.int32)[:, None]
    ).astype(f32)
    return jnp.matmul(x, expand, precision=lax.Precision.HIGHEST)


def grid_pairs(n, side, along, shift):
    pairs = []
    for k in range(n):
        row, col = divmod(k, side)
        if along == "x":
            dst = row * side + (col + shift) % side
        else:
            dst = ((row + shift) % side) * side + col
        pairs.append((k, dst))
    return pairs


def ring_gather(x, n, side, along):
    assert side == 4
    from_left = lax.ppermute(x, "seq", grid_pairs(n, side, along, 1))
    from_right = lax.ppermute(x, "seq", grid_pairs(n, side, along, -1))
    half = x.shape[-2] // 2
    far_a = lax.ppermute(from_left[..., :half, :], "seq", grid_pairs(n, side, along, 1))
    far_b = lax.ppermute(from_right[..., half:, :], "seq", grid_pairs(n, side, along, -1))
    far = jnp.concatenate([far_a, far_b], axis=-2)
    return jnp.stack([x, from_right, far, from_left], 0)


def conv_rows(ext, ext_doc, out_doc, conv_weight, conv_bias):
    rows = out_doc.shape[-1]
    accum = jnp.zeros(ext.shape[:-2] + (rows, CHANNELS), f32) + conv_bias
    for offset in range(KERNEL):
        keep = (ext_doc[..., offset : offset + rows] == out_doc).astype(f32)
        accum = (
            accum
            + conv_weight[offset]
            * ext[..., offset : offset + rows, :].astype(f32)
            * keep[..., None]
        )
    return jax.nn.silu(accum).astype(bf16)


def body(
    mixer_in,
    gate_input,
    step_raw,
    lengths,
    deal_order,
    conv_weight,
    conv_bias,
    step_bias,
    decay_rate,
    skip_gain,
    norm_gain,
):
    n = deal_order.shape[0]
    docs = lengths.shape[0]
    me = lax.axis_index("seq")
    rows_here = INNER // n
    mine = deal_order[me]
    ends = jnp.cumsum(lengths).astype(jnp.int32)
    lane = jnp.arange(STRETCH, dtype=jnp.int32)
    doc = doc_index(ends, mine * STRETCH + lane)
    end_doc_mine = doc[-1]

    step = jax.nn.softplus(step_raw.astype(f32) + step_bias)
    log_decay = -decay_rate * step
    lc = jnp.cumsum(log_decay, axis=0)
    total = lc[-1]

    ext_local = jnp.concatenate([jnp.zeros((LEAD, CHANNELS), bf16), mixer_in], 0)
    ext_doc_local = jnp.concatenate([jnp.full((LEAD,), -1, jnp.int32), doc], 0)
    mixed_local = conv_rows(ext_local, ext_doc_local, doc, conv_weight, conv_bias)
    scaled_local = (
        mixed_local[:, :INNER].astype(f32) * per_head(step)
    ).astype(bf16)
    keys_local = mixed_local[:, INNER : INNER + STATE]
    weight_end = jnp.where(
        ((doc == end_doc_mine) & (lane >= LEAD))[:, None], jnp.exp(total[None, :] - lc), 0.0
    )
    weighted_local = (scaled_local.astype(f32) * per_head(weight_end)).astype(bf16)
    state_part = jnp.dot(weighted_local.T, keys_local, preferred_element_type=f32)

    doc_last = ends - 1
    doc_owner = doc_last // STRETCH
    doc_at = doc_last - doc_owner * STRETCH
    lc_at_end = jnp.where(
        (doc_owner == mine)[:, None], lc[jnp.clip(doc_at, 0, STRETCH - 1)], 0.0
    )
    w_lead = jnp.where(
        (doc[:LEAD] == end_doc_mine)[:, None], jnp.exp(total[None, :] - lc[:LEAD]), 0.0
    )
    edge_rows = jnp.concatenate([mixer_in[:LEAD], mixer_in[STRETCH - LEAD :]], 0).astype(f32)
    pieces = [
        edge_rows.reshape(-1),
        total,
        step[:LEAD].reshape(-1),
        w_lead.reshape(-1),
        lc_at_end.reshape(-1),
    ]
    flat = jnp.concatenate(pieces)
    width = flat.shape[0]
    padded_width = -(-width // 128) * 128
    flat = jnp.pad(flat, (0, padded_width - width))
    split = INNER // 2
    state_bf = state_part.astype(bf16)
    flat, send_a, send_b = lax.optimization_barrier((flat, state_bf[:split], state_bf[split:]))
    side = 4
    assert side * side == n
    gathered_a = ring_gather(ring_gather(send_a, n, side, "x"), n, side, "y").reshape(n, split, STATE)
    gathered_b = ring_gather(ring_gather(send_b, n, side, "y"), n, side, "x").reshape(n, split, STATE)
    my_row, my_col = me // side, me % side
    offs = jnp.arange(side, dtype=jnp.int32)
    order_a = (
        ((my_row + offs[:, None]) % side) * side + (my_col + offs[None, :]) % side
    ).reshape(-1)
    order_b = (
        ((my_row + offs[None, :]) % side) * side + (my_col + offs[:, None]) % side
    ).reshape(-1)
    small = lax.all_to_all(
        jnp.broadcast_to(flat[None], (n, padded_width)), "seq", 0, 0, tiled=True
    )

    slots = jnp.arange(n, dtype=jnp.int32)
    holder = jnp.sum(
        jnp.where(deal_order[None, :] == slots[:, None], slots[None, :], 0), axis=1
    )
    seq_small = jnp.take(small, holder, axis=0)
    cursor = 0
    sizes = [2 * LEAD * CHANNELS, HEADS, LEAD * HEADS, LEAD * HEADS, docs * HEADS]
    cut = []
    for size in sizes:
        cut.append((cursor, cursor + size))
        cursor += size
    edge_seq = seq_small[:, cut[0][0] : cut[0][1]].reshape(n, 2 * LEAD, CHANNELS)
    totals_seq = seq_small[:, cut[1][0] : cut[1][1]]
    step_lead_seq = seq_small[:, cut[2][0] : cut[2][1]].reshape(n, LEAD, HEADS)
    w_lead_seq = seq_small[:, cut[3][0] : cut[3][1]].reshape(n, LEAD, HEADS)
    lc_end = jnp.sum(small[:, cut[4][0] : cut[4][1]], axis=0).reshape(docs, HEADS)

    head_seq = edge_seq[:, :LEAD].astype(bf16)
    tail_seq = edge_seq[:, LEAD:].astype(bf16)
    prev_tail = jnp.concatenate([jnp.zeros((1, LEAD, CHANNELS), bf16), tail_seq[:-1]], 0)
    ext6 = jnp.concatenate([prev_tail, head_seq], 1)
    ext6_pos = slots[:, None] * STRETCH - LEAD + jnp.arange(2 * LEAD, dtype=jnp.int32)[None, :]
    ext6_doc = jnp.where(ext6_pos >= 0, doc_index(ends, ext6_pos), -1)
    lead_doc = ext6_doc[:, LEAD:]
    mixed_lead = conv_rows(ext6, ext6_doc, lead_doc, conv_weight, conv_bias)
    scaled_lead = (mixed_lead[..., :INNER].astype(f32) * per_head(step_lead_seq)).astype(bf16)
    keys_lead = mixed_lead[..., INNER : INNER + STATE]
    weighted_lead = (scaled_lead.astype(f32) * per_head(w_lead_seq)).astype(bf16)

    mixed = jnp.concatenate([mixed_lead[mine], mixed_local[LEAD:]], 0)
    values = mixed[:, :INNER]
    keys = mixed[:, INNER : INNER + STATE]
    queries = mixed[:, INNER + STATE :]
    scaled = (values.astype(f32) * per_head(step)).astype(bf16)

    end_doc_seq = doc_index(ends, slots * STRETCH + STRETCH - 1)
    prev_seq = jnp.where(slots > 0, doc_index(ends, slots * STRETCH - 1), -1)
    between = (slots[None, :, None] < slots[None, None, :]) & (
        slots[None, None, :] < slots[:, None, None]
    )
    gap = jnp.sum(jnp.where(between[..., None], totals_seq[None, None], 0.0), axis=2)
    allowed = (slots[None, :] < slots[:, None]) & (end_doc_seq[None, :] == prev_seq[:, None])
    cross = jnp.where(allowed[..., None], jnp.exp(gap), 0.0)
    cross_dev = jnp.take(cross, deal_order, axis=1)

    receivers = jnp.concatenate([mine[None], doc_owner])
    recv_cross = cross[receivers]
    lead_mix = (
        per_head(recv_cross)[:, :, None, :] * weighted_lead.astype(f32)[None]
    ).reshape(receivers.shape[0], n * LEAD, INNER)
    lead_state = jnp.einsum(
        "rxk,xn->rkn",
        lead_mix,
        keys_lead.reshape(n * LEAD, STATE).astype(f32),
        precision=lax.Precision.HIGHEST,
    )

    scores = jnp.dot(queries, keys.T, preferred_element_type=f32)
    later = lane[:, None] >= lane[None, :]
    same = (doc[:, None] == doc[None, :]) & later
    spans = lc.T[:, :, None] - lc.T[:, None, :]
    mixing = (scores[None] * jnp.exp(jnp.where(same[None], spans, -jnp.inf))).astype(bf16)
    within = jnp.einsum(
        "hts,shp->thp",
        mixing,
        scaled.reshape(STRETCH, HEADS, HEAD_DIM),
        preferred_element_type=f32,
    ).reshape(STRETCH, INNER)
    direct = values.astype(f32) * per_head(skip_gain)[None, :]

    doc_ids = jnp.arange(docs, dtype=jnp.int32)
    lc_own_end = lc[jnp.clip(doc_at, 0, STRETCH - 1)]
    final_weight = jnp.where(
        ((doc[None, :] == doc_ids[:, None]) & (doc_owner == mine)[:, None])[..., None],
        jnp.exp(lc_own_end[:, None, :] - lc[None]),
        0.0,
    )
    final_weighted = (scaled.astype(f32)[None] * per_head(final_weight)).astype(bf16)
    final_part = jnp.einsum(
        "dsk,sn->dkn", final_weighted, keys, preferred_element_type=f32
    ).astype(bf16)
    if FINAL_VIA_ALL_TO_ALL:
        parts_in = lax.all_to_all(
            final_part.reshape(docs, n, rows_here, STATE), "seq", 1, 1, tiled=True
        )
        part_here = jnp.sum(parts_in.astype(f32), axis=1)
    else:
        part_here = jnp.transpose(
            lax.psum_scatter(
                jnp.transpose(final_part, (1, 0, 2)), "seq", scatter_dimension=0, tiled=True
            ),
            (1, 0, 2),
        ).astype(f32)

    own_w = per_head(cross_dev[mine])
    w_a = jnp.take(own_w, order_a, axis=0)[:, :split]
    w_b = jnp.take(own_w, order_b, axis=0)[:, split:]
    state_a = lead_state[0][:split]
    state_b = lead_state[0][split:]
    for k in range(n):
        state_a = state_a + w_a[k][:, None] * gathered_a[k].astype(f32)
        state_b = state_b + w_b[k][:, None] * gathered_b[k].astype(f32)
    state_in = jnp.concatenate([state_a, state_b], 0)
    readout = jnp.dot(queries, state_in.astype(bf16).T, preferred_element_type=f32)
    carry_weight = jnp.exp(jnp.where((doc == prev_seq[mine])[:, None], lc, -jnp.inf))
    outputs = within + readout * per_head(carry_weight) + direct
    gated = outputs * jax.nn.silu(gate_input.astype(f32))
    normed = gated * lax.rsqrt(jnp.mean(gated * gated, axis=1, keepdims=True) + 1e-05) * norm_gain
    mixed_out = normed.astype(bf16)

    row_ids = me * rows_here + jnp.arange(rows_here, dtype=jnp.int32)
    row_head = row_ids // HEAD_DIM
    first_row = me * rows_here
    in_a = first_row < split
    rows_a = lax.dynamic_slice_in_dim(
        gathered_a, jnp.clip(first_row, 0, split - rows_here), rows_here, axis=1
    )
    rows_b = lax.dynamic_slice_in_dim(
        gathered_b, jnp.clip(first_row - split, 0, INNER - split - rows_here), rows_here, axis=1
    )
    gs_rows = jnp.where(in_a, rows_a, rows_b).astype(f32)
    source_order = jnp.where(in_a, order_a, order_b)
    owner_cross = jnp.take(cross_dev[doc_owner], source_order, axis=1)[:, :, row_head]
    owner_in = jnp.einsum("dkr,krn->drn", owner_cross, gs_rows, precision=lax.Precision.HIGHEST)
    owner_in = owner_in + lax.dynamic_slice_in_dim(lead_state[1:], me * rows_here, rows_here, axis=1)
    carry_final = jnp.where(
        (prev_seq[doc_owner] == doc_ids)[:, None], jnp.exp(lc_end[:, row_head]), 0.0
    )
    final_states = part_here + carry_final[..., None] * owner_in
    return (mixed_out, final_states)


def solution(mesh):
    return jax.shard_map(
        body,
        mesh=mesh,
        in_specs=(
            P(("dp", "seq"), None),
            P(("dp", "seq"), None),
            P(("dp", "seq"), None),
            P("dp"),
            P("dp"),
            P(),
            P(),
            P(),
            P(),
            P(),
            P(),
        ),
        out_specs=(P(("dp", "seq"), None), P("dp", "seq", None)),
        check_vma=False,
    )
```

```python
import jax
import jax.numpy as jnp
from jax import lax
from jax.sharding import PartitionSpec as P

HEADS = 40
HEAD_DIM = 64
STATE = 128
KERNEL = 4
STRETCH = 256
INNER = 2560
CHANNELS = 2816
LEAD = KERNEL - 1
LONGEST = 2048
FINAL_VIA_ALL_TO_ALL = True

f32 = jnp.float32
bf16 = jnp.bfloat16


def doc_index(ends, positions):
    return jnp.sum((ends[None, :] <= positions[..., None]).astype(jnp.int32), axis=-1)


def per_head(x):
    expand = (
        jnp.arange(HEADS * HEAD_DIM, dtype=jnp.int32)[None, :] // HEAD_DIM
        == jnp.arange(HEADS, dtype=jnp.int32)[:, None]
    ).astype(f32)
    return jnp.matmul(x, expand, precision=lax.Precision.HIGHEST)


def conv_rows(ext, ext_doc, out_doc, conv_weight, conv_bias):
    rows = out_doc.shape[-1]
    accum = jnp.zeros(ext.shape[:-2] + (rows, CHANNELS), f32) + conv_bias
    for offset in range(KERNEL):
        keep = (ext_doc[..., offset : offset + rows] == out_doc).astype(f32)
        accum = (
            accum
            + conv_weight[offset]
            * ext[..., offset : offset + rows, :].astype(f32)
            * keep[..., None]
        )
    return jax.nn.silu(accum).astype(bf16)


def body(
    mixer_in,
    gate_input,
    step_raw,
    lengths,
    deal_order,
    conv_weight,
    conv_bias,
    step_bias,
    decay_rate,
    skip_gain,
    norm_gain,
):
    n = deal_order.shape[0]
    docs = lengths.shape[0]
    me = lax.axis_index("seq")
    rows_here = INNER // n
    mine = deal_order[me]
    ends = jnp.cumsum(lengths).astype(jnp.int32)
    lane = jnp.arange(STRETCH, dtype=jnp.int32)
    doc = doc_index(ends, mine * STRETCH + lane)
    end_doc_mine = doc[-1]

    step = jax.nn.softplus(step_raw.astype(f32) + step_bias)
    log_decay = -decay_rate * step
    lc = jnp.cumsum(log_decay, axis=0)
    total = lc[-1]

    ext_local = jnp.concatenate([jnp.zeros((LEAD, CHANNELS), bf16), mixer_in], 0)
    ext_doc_local = jnp.concatenate([jnp.full((LEAD,), -1, jnp.int32), doc], 0)
    mixed_local = conv_rows(ext_local, ext_doc_local, doc, conv_weight, conv_bias)
    scaled_local = (
        mixed_local[:, :INNER].astype(f32) * per_head(step)
    ).astype(bf16)
    keys_local = mixed_local[:, INNER : INNER + STATE]
    weight_end = jnp.where(
        ((doc == end_doc_mine) & (lane >= LEAD))[:, None], jnp.exp(total[None, :] - lc), 0.0
    )
    weighted_local = (scaled_local.astype(f32) * per_head(weight_end)).astype(bf16)
    state_part = jnp.dot(weighted_local.T, keys_local, preferred_element_type=f32)

    doc_last = ends - 1
    doc_owner = doc_last // STRETCH
    doc_at = doc_last - doc_owner * STRETCH
    lc_at_end = jnp.where(
        (doc_owner == mine)[:, None], lc[jnp.clip(doc_at, 0, STRETCH - 1)], 0.0
    )
    w_lead = jnp.where(
        (doc[:LEAD] == end_doc_mine)[:, None], jnp.exp(total[None, :] - lc[:LEAD]), 0.0
    )
    edge_rows = jnp.concatenate([mixer_in[:LEAD], mixer_in[STRETCH - LEAD :]], 0).astype(f32)
    pieces = [
        edge_rows.reshape(-1),
        total,
        step[:LEAD].reshape(-1),
        w_lead.reshape(-1),
        lc_at_end.reshape(-1),
    ]
    flat = jnp.concatenate(pieces)
    width = flat.shape[0]
    padded_width = -(-width // 128) * 128
    flat = jnp.pad(flat, (0, padded_width - width))
    flat, state_send = lax.optimization_barrier((flat, state_part.astype(bf16)))
    gathered_states = lax.all_gather(state_send, "seq", axis=0, tiled=False)
    small = lax.all_to_all(
        jnp.broadcast_to(flat[None], (n, padded_width)), "seq", 0, 0, tiled=True
    )

    slots = jnp.arange(n, dtype=jnp.int32)
    holder = jnp.sum(
        jnp.where(deal_order[None, :] == slots[:, None], slots[None, :], 0), axis=1
    )
    seq_small = jnp.take(small, holder, axis=0)
    cursor = 0
    sizes = [2 * LEAD * CHANNELS, HEADS, LEAD * HEADS, LEAD * HEADS, docs * HEADS]
    cut = []
    for size in sizes:
        cut.append((cursor, cursor + size))
        cursor += size
    edge_seq = seq_small[:, cut[0][0] : cut[0][1]].reshape(n, 2 * LEAD, CHANNELS)
    totals_seq = seq_small[:, cut[1][0] : cut[1][1]]
    step_lead_seq = seq_small[:, cut[2][0] : cut[2][1]].reshape(n, LEAD, HEADS)
    w_lead_seq = seq_small[:, cut[3][0] : cut[3][1]].reshape(n, LEAD, HEADS)
    lc_end = jnp.sum(small[:, cut[4][0] : cut[4][1]], axis=0).reshape(docs, HEADS)

    head_seq = edge_seq[:, :LEAD].astype(bf16)
    tail_seq = edge_seq[:, LEAD:].astype(bf16)
    prev_tail = jnp.concatenate([jnp.zeros((1, LEAD, CHANNELS), bf16), tail_seq[:-1]], 0)
    ext6 = jnp.concatenate([prev_tail, head_seq], 1)
    ext6_pos = slots[:, None] * STRETCH - LEAD + jnp.arange(2 * LEAD, dtype=jnp.int32)[None, :]
    ext6_doc = jnp.where(ext6_pos >= 0, doc_index(ends, ext6_pos), -1)
    lead_doc = ext6_doc[:, LEAD:]
    mixed_lead = conv_rows(ext6, ext6_doc, lead_doc, conv_weight, conv_bias)
    scaled_lead = (mixed_lead[..., :INNER].astype(f32) * per_head(step_lead_seq)).astype(bf16)
    keys_lead = mixed_lead[..., INNER : INNER + STATE]
    weighted_lead = (scaled_lead.astype(f32) * per_head(w_lead_seq)).astype(bf16)

    mixed = jnp.concatenate([mixed_lead[mine], mixed_local[LEAD:]], 0)
    values = mixed[:, :INNER]
    keys = mixed[:, INNER : INNER + STATE]
    queries = mixed[:, INNER + STATE :]
    scaled = (values.astype(f32) * per_head(step)).astype(bf16)

    end_doc_seq = doc_index(ends, slots * STRETCH + STRETCH - 1)
    prev_seq = jnp.where(slots > 0, doc_index(ends, slots * STRETCH - 1), -1)
    between = (slots[None, :, None] < slots[None, None, :]) & (
        slots[None, None, :] < slots[:, None, None]
    )
    gap = jnp.sum(jnp.where(between[..., None], totals_seq[None, None], 0.0), axis=2)
    allowed = (slots[None, :] < slots[:, None]) & (end_doc_seq[None, :] == prev_seq[:, None])
    cross = jnp.where(allowed[..., None], jnp.exp(gap), 0.0)
    cross_dev = jnp.take(cross, deal_order, axis=1)

    receivers = jnp.concatenate([mine[None], doc_owner])
    recv_cross = cross[receivers]
    lead_mix = (
        per_head(recv_cross)[:, :, None, :] * weighted_lead.astype(f32)[None]
    ).reshape(receivers.shape[0], n * LEAD, INNER)
    lead_state = jnp.einsum(
        "rxk,xn->rkn",
        lead_mix,
        keys_lead.reshape(n * LEAD, STATE).astype(f32),
        precision=lax.Precision.HIGHEST,
    )

    scores = jnp.dot(queries, keys.T, preferred_element_type=f32)
    later = lane[:, None] >= lane[None, :]
    same = (doc[:, None] == doc[None, :]) & later
    spans = lc.T[:, :, None] - lc.T[:, None, :]
    mixing = (scores[None] * jnp.exp(jnp.where(same[None], spans, -jnp.inf))).astype(bf16)
    within = jnp.einsum(
        "hts,shp->thp",
        mixing,
        scaled.reshape(STRETCH, HEADS, HEAD_DIM),
        preferred_element_type=f32,
    ).reshape(STRETCH, INNER)
    direct = values.astype(f32) * per_head(skip_gain)[None, :]

    doc_ids = jnp.arange(docs, dtype=jnp.int32)
    lc_own_end = lc[jnp.clip(doc_at, 0, STRETCH - 1)]
    final_weight = jnp.where(
        ((doc[None, :] == doc_ids[:, None]) & (doc_owner == mine)[:, None])[..., None],
        jnp.exp(lc_own_end[:, None, :] - lc[None]),
        0.0,
    )
    final_weighted = (scaled.astype(f32)[None] * per_head(final_weight)).astype(bf16)
    final_part = jnp.einsum(
        "dsk,sn->dkn", final_weighted, keys, preferred_element_type=f32
    ).astype(bf16)
    if FINAL_VIA_ALL_TO_ALL:
        parts_in = lax.all_to_all(
            final_part.reshape(docs, n, rows_here, STATE), "seq", 1, 1, tiled=True
        )
        part_here = jnp.sum(parts_in.astype(f32), axis=1)
    else:
        part_here = jnp.transpose(
            lax.psum_scatter(
                jnp.transpose(final_part, (1, 0, 2)), "seq", scatter_dimension=0, tiled=True
            ),
            (1, 0, 2),
        ).astype(f32)

    reach = min(LONGEST // STRETCH, n)
    back = mine - 1 - jnp.arange(reach, dtype=jnp.int32)
    back_ok = back >= 0
    back_c = jnp.clip(back, 0, n - 1)
    near_w = per_head(jnp.where(back_ok[:, None], cross[mine][back_c], 0.0))
    near_src = holder[back_c]
    state_in = lead_state[0]
    for i in range(reach):
        near_state = lax.dynamic_index_in_dim(gathered_states, near_src[i], axis=0, keepdims=False)
        state_in = state_in + near_w[i][:, None] * near_state.astype(f32)
    readout = jnp.dot(queries, state_in.astype(bf16).T, preferred_element_type=f32)
    carry_weight = jnp.exp(jnp.where((doc == prev_seq[mine])[:, None], lc, -jnp.inf))
    outputs = within + readout * per_head(carry_weight) + direct
    gated = outputs * jax.nn.silu(gate_input.astype(f32))
    normed = gated * lax.rsqrt(jnp.mean(gated * gated, axis=1, keepdims=True) + 1e-05) * norm_gain
    mixed_out = normed.astype(bf16)

    row_ids = me * rows_here + jnp.arange(rows_here, dtype=jnp.int32)
    row_head = row_ids // HEAD_DIM
    gs_rows = lax.dynamic_slice_in_dim(
        gathered_states, me * rows_here, rows_here, axis=1
    ).astype(f32)
    owner_cross = cross_dev[doc_owner][:, :, row_head]
    owner_in = jnp.einsum("dkr,krn->drn", owner_cross, gs_rows, precision=lax.Precision.HIGHEST)
    owner_in = owner_in + lax.dynamic_slice_in_dim(lead_state[1:], me * rows_here, rows_here, axis=1)
    carry_final = jnp.where(
        (prev_seq[doc_owner] == doc_ids)[:, None], jnp.exp(lc_end[:, row_head]), 0.0
    )
    final_states = part_here + carry_final[..., None] * owner_in
    return (mixed_out, final_states)


def solution(mesh):
    return jax.shard_map(
        body,
        mesh=mesh,
        in_specs=(
            P(("dp", "seq"), None),
            P(("dp", "seq"), None),
            P(("dp", "seq"), None),
            P("dp"),
            P("dp"),
            P(),
            P(),
            P(),
            P(),
            P(),
            P(),
        ),
        out_specs=(P(("dp", "seq"), None), P("dp", "seq", None)),
        check_vma=False,
    )
```

```python
import jax
import jax.numpy as jnp
from jax import lax
from jax.sharding import PartitionSpec as P

HEADS = 40
HEAD_DIM = 64
STATE = 128
KERNEL = 4
STRETCH = 256
INNER = 2560
CHANNELS = 2816
LEAD = KERNEL - 1
LONGEST = 2048
FINAL_VIA_ALL_TO_ALL = True

f32 = jnp.float32
bf16 = jnp.bfloat16


def doc_index(ends, positions):
    return jnp.sum((ends[None, :] <= positions[..., None]).astype(jnp.int32), axis=-1)


def per_head(x):
    expand = (
        jnp.arange(HEADS * HEAD_DIM, dtype=jnp.int32)[None, :] // HEAD_DIM
        == jnp.arange(HEADS, dtype=jnp.int32)[:, None]
    ).astype(f32)
    return jnp.matmul(x, expand, precision=lax.Precision.HIGHEST)


def conv_rows(ext, ext_doc, out_doc, conv_weight, conv_bias):
    rows = out_doc.shape[-1]
    accum = jnp.zeros(ext.shape[:-2] + (rows, CHANNELS), f32) + conv_bias
    for offset in range(KERNEL):
        keep = (ext_doc[..., offset : offset + rows] == out_doc).astype(f32)
        accum = (
            accum
            + conv_weight[offset]
            * ext[..., offset : offset + rows, :].astype(f32)
            * keep[..., None]
        )
    return jax.nn.silu(accum).astype(bf16)


def body(
    mixer_in,
    gate_input,
    step_raw,
    lengths,
    deal_order,
    conv_weight,
    conv_bias,
    step_bias,
    decay_rate,
    skip_gain,
    norm_gain,
):
    n = deal_order.shape[0]
    docs = lengths.shape[0]
    me = lax.axis_index("seq")
    rows_here = INNER // n
    mine = deal_order[me]
    ends = jnp.cumsum(lengths).astype(jnp.int32)
    lane = jnp.arange(STRETCH, dtype=jnp.int32)
    doc = doc_index(ends, mine * STRETCH + lane)
    end_doc_mine = doc[-1]

    step = jax.nn.softplus(step_raw.astype(f32) + step_bias)
    log_decay = -decay_rate * step
    lc = jnp.cumsum(log_decay, axis=0)
    total = lc[-1]

    ext_local = jnp.concatenate([jnp.zeros((LEAD, CHANNELS), bf16), mixer_in], 0)
    ext_doc_local = jnp.concatenate([jnp.full((LEAD,), -1, jnp.int32), doc], 0)
    mixed_local = conv_rows(ext_local, ext_doc_local, doc, conv_weight, conv_bias)
    scaled_local = (
        mixed_local[:, :INNER].astype(f32) * per_head(step)
    ).astype(bf16)
    keys_local = mixed_local[:, INNER : INNER + STATE]
    weight_end = jnp.where(
        ((doc == end_doc_mine) & (lane >= LEAD))[:, None], jnp.exp(total[None, :] - lc), 0.0
    )
    weighted_local = (scaled_local.astype(f32) * per_head(weight_end)).astype(bf16)
    state_part = jnp.dot(weighted_local.T, keys_local, preferred_element_type=f32)

    edge_raw = jnp.concatenate([mixer_in[:LEAD], mixer_in[STRETCH - LEAD :]], 0)
    state_send, lc_b, step_b, edge_b = lax.optimization_barrier(
        (state_part.astype(bf16), lc, step, edge_raw)
    )
    gathered_states = lax.all_gather(state_send, "seq", axis=0, tiled=False)
    total_b = lc_b[-1]
    doc_last = ends - 1
    doc_owner = doc_last // STRETCH
    doc_at = doc_last - doc_owner * STRETCH
    lc_at_end = jnp.where(
        (doc_owner == mine)[:, None], lc_b[jnp.clip(doc_at, 0, STRETCH - 1)], 0.0
    )
    w_lead = jnp.where(
        (doc[:LEAD] == end_doc_mine)[:, None], jnp.exp(total_b[None, :] - lc_b[:LEAD]), 0.0
    )
    pieces = [
        edge_b.astype(f32).reshape(-1),
        total_b,
        step_b[:LEAD].reshape(-1),
        w_lead.reshape(-1),
        lc_at_end.reshape(-1),
    ]
    flat = jnp.concatenate(pieces)
    width = flat.shape[0]
    padded_width = -(-width // 128) * 128
    flat = jnp.pad(flat, (0, padded_width - width))
    small = lax.all_to_all(
        jnp.broadcast_to(flat[None], (n, padded_width)), "seq", 0, 0, tiled=True
    )

    slots = jnp.arange(n, dtype=jnp.int32)
    holder = jnp.sum(
        jnp.where(deal_order[None, :] == slots[:, None], slots[None, :], 0), axis=1
    )
    seq_small = jnp.take(small, holder, axis=0)
    cursor = 0
    sizes = [2 * LEAD * CHANNELS, HEADS, LEAD * HEADS, LEAD * HEADS, docs * HEADS]
    cut = []
    for size in sizes:
        cut.append((cursor, cursor + size))
        cursor += size
    edge_seq = seq_small[:, cut[0][0] : cut[0][1]].reshape(n, 2 * LEAD, CHANNELS)
    totals_seq = seq_small[:, cut[1][0] : cut[1][1]]
    step_lead_seq = seq_small[:, cut[2][0] : cut[2][1]].reshape(n, LEAD, HEADS)
    w_lead_seq = seq_small[:, cut[3][0] : cut[3][1]].reshape(n, LEAD, HEADS)
    lc_end = jnp.sum(small[:, cut[4][0] : cut[4][1]], axis=0).reshape(docs, HEADS)

    head_seq = edge_seq[:, :LEAD].astype(bf16)
    tail_seq = edge_seq[:, LEAD:].astype(bf16)
    prev_tail = jnp.concatenate([jnp.zeros((1, LEAD, CHANNELS), bf16), tail_seq[:-1]], 0)
    ext6 = jnp.concatenate([prev_tail, head_seq], 1)
    ext6_pos = slots[:, None] * STRETCH - LEAD + jnp.arange(2 * LEAD, dtype=jnp.int32)[None, :]
    ext6_doc = jnp.where(ext6_pos >= 0, doc_index(ends, ext6_pos), -1)
    lead_doc = ext6_doc[:, LEAD:]
    mixed_lead = conv_rows(ext6, ext6_doc, lead_doc, conv_weight, conv_bias)
    scaled_lead = (mixed_lead[..., :INNER].astype(f32) * per_head(step_lead_seq)).astype(bf16)
    keys_lead = mixed_lead[..., INNER : INNER + STATE]
    weighted_lead = (scaled_lead.astype(f32) * per_head(w_lead_seq)).astype(bf16)

    mixed = jnp.concatenate([mixed_lead[mine], mixed_local[LEAD:]], 0)
    values = mixed[:, :INNER]
    keys = mixed[:, INNER : INNER + STATE]
    queries = mixed[:, INNER + STATE :]
    scaled = (values.astype(f32) * per_head(step)).astype(bf16)

    end_doc_seq = doc_index(ends, slots * STRETCH + STRETCH - 1)
    prev_seq = jnp.where(slots > 0, doc_index(ends, slots * STRETCH - 1), -1)
    between = (slots[None, :, None] < slots[None, None, :]) & (
        slots[None, None, :] < slots[:, None, None]
    )
    gap = jnp.sum(jnp.where(between[..., None], totals_seq[None, None], 0.0), axis=2)
    allowed = (slots[None, :] < slots[:, None]) & (end_doc_seq[None, :] == prev_seq[:, None])
    cross = jnp.where(allowed[..., None], jnp.exp(gap), 0.0)
    cross_dev = jnp.take(cross, deal_order, axis=1)

    receivers = jnp.concatenate([mine[None], doc_owner])
    recv_cross = cross[receivers]
    lead_mix = (
        per_head(recv_cross)[:, :, None, :] * weighted_lead.astype(f32)[None]
    ).reshape(receivers.shape[0], n * LEAD, INNER)
    lead_state = jnp.einsum(
        "rxk,xn->rkn",
        lead_mix,
        keys_lead.reshape(n * LEAD, STATE).astype(f32),
        precision=lax.Precision.HIGHEST,
    )

    scores = jnp.dot(queries, keys.T, preferred_element_type=f32)
    later = lane[:, None] >= lane[None, :]
    same = (doc[:, None] == doc[None, :]) & later
    spans = lc.T[:, :, None] - lc.T[:, None, :]
    mixing = (scores[None] * jnp.exp(jnp.where(same[None], spans, -jnp.inf))).astype(bf16)
    within = jnp.einsum(
        "hts,shp->thp",
        mixing,
        scaled.reshape(STRETCH, HEADS, HEAD_DIM),
        preferred_element_type=f32,
    ).reshape(STRETCH, INNER)
    direct = values.astype(f32) * per_head(skip_gain)[None, :]

    doc_ids = jnp.arange(docs, dtype=jnp.int32)
    lc_own_end = lc[jnp.clip(doc_at, 0, STRETCH - 1)]
    final_weight = jnp.where(
        ((doc[None, :] == doc_ids[:, None]) & (doc_owner == mine)[:, None])[..., None],
        jnp.exp(lc_own_end[:, None, :] - lc[None]),
        0.0,
    )
    final_weighted = (scaled.astype(f32)[None] * per_head(final_weight)).astype(bf16)
    final_part = jnp.einsum(
        "dsk,sn->dkn", final_weighted, keys, preferred_element_type=f32
    ).astype(bf16)
    if FINAL_VIA_ALL_TO_ALL:
        parts_in = lax.all_to_all(
            final_part.reshape(docs, n, rows_here, STATE), "seq", 1, 1, tiled=True
        )
        part_here = jnp.sum(parts_in.astype(f32), axis=1)
    else:
        part_here = jnp.transpose(
            lax.psum_scatter(
                jnp.transpose(final_part, (1, 0, 2)), "seq", scatter_dimension=0, tiled=True
            ),
            (1, 0, 2),
        ).astype(f32)

    reach = min(LONGEST // STRETCH, n)
    back = mine - 1 - jnp.arange(reach, dtype=jnp.int32)
    back_ok = back >= 0
    back_c = jnp.clip(back, 0, n - 1)
    near_w = per_head(jnp.where(back_ok[:, None], cross[mine][back_c], 0.0))
    near_src = holder[back_c]
    state_in = lead_state[0]
    for i in range(reach):
        near_state = lax.dynamic_index_in_dim(gathered_states, near_src[i], axis=0, keepdims=False)
        state_in = state_in + near_w[i][:, None] * near_state.astype(f32)
    readout = jnp.dot(queries, state_in.astype(bf16).T, preferred_element_type=f32)
    carry_weight = jnp.exp(jnp.where((doc == prev_seq[mine])[:, None], lc, -jnp.inf))
    outputs = within + readout * per_head(carry_weight) + direct
    gated = outputs * jax.nn.silu(gate_input.astype(f32))
    normed = gated * lax.rsqrt(jnp.mean(gated * gated, axis=1, keepdims=True) + 1e-05) * norm_gain
    mixed_out = normed.astype(bf16)

    row_ids = me * rows_here + jnp.arange(rows_here, dtype=jnp.int32)
    row_head = row_ids // HEAD_DIM
    gs_rows = lax.dynamic_slice_in_dim(
        gathered_states, me * rows_here, rows_here, axis=1
    ).astype(f32)
    owner_cross = cross_dev[doc_owner][:, :, row_head]
    owner_in = jnp.einsum("dkr,krn->drn", owner_cross, gs_rows, precision=lax.Precision.HIGHEST)
    owner_in = owner_in + lax.dynamic_slice_in_dim(lead_state[1:], me * rows_here, rows_here, axis=1)
    carry_final = jnp.where(
        (prev_seq[doc_owner] == doc_ids)[:, None], jnp.exp(lc_end[:, row_head]), 0.0
    )
    final_states = part_here + carry_final[..., None] * owner_in
    return (mixed_out, final_states)


def solution(mesh):
    return jax.shard_map(
        body,
        mesh=mesh,
        in_specs=(
            P(("dp", "seq"), None),
            P(("dp", "seq"), None),
            P(("dp", "seq"), None),
            P("dp"),
            P("dp"),
            P(),
            P(),
            P(),
            P(),
            P(),
            P(),
        ),
        out_specs=(P(("dp", "seq"), None), P("dp", "seq", None)),
        check_vma=False,
    )
```
